256 devices in a mesh: seq: 16 (over x, y), grp: 16 (over z, core).
Axes of the slice: x: 4, y: 4, z: 8, core: 2. Of those that a mesh axis runs over, the one named last changes fastest.
Arguments:
- query_rows: bfloat16 [16, 2048, 4096], P('grp', 'seq'), may hold values from -6 to 6
- key_rows: bfloat16 [16, 2048, 1024], P('grp', 'seq'), may hold values from -6 to 6
- value_rows: bfloat16 [16, 2048, 1024], P('grp', 'seq'), may hold values from -27 to 27
- doc_of_block: int32 [16, 16], P('grp'), may hold values from 0 to 3, never falling along the last dimension, each value on 1 to 8 neighbouring positions
- expert_ids: int32 [16, 2048, 2], P('grp', 'seq'), may hold values from 0 to 7, as said below
- gate_weights: float32 [16, 2048, 2], P('grp', 'seq'), may hold values from 0.1 to 0.9
- norm_gain: float32 [4096], replicated, may hold values from 0.1 to 1.9
- w_in: bfloat16 [2, 7168, 4096], P(None, ('seq', 'grp')), may hold values from -0.09375 to 0.09375
- w_down: bfloat16 [7168, 4096], P(('seq', 'grp')), may hold values from -0.0625 to 0.0625
Outputs:
- layer_out: bfloat16 [16, 2048, 4096], P('grp', 'seq')
The draws below stay inside these ranges and needn't reach their ends.
Inputs may be any that keep to these rules, and one draw needn't show every extreme that they name: `expert_ids`: each token names 2 different experts; in each aligned block of 128 tokens along a sequence (the tokens of one device) at most 40 tokens name expert 0, and in every draw some block has exactly 40 such tokens.
All inputs are finite; a program needn't handle non-finite values.
Results may differ from the reference program's by a relative error of at most 0.014.
Values may be sent and summed in bfloat16 or wider, within the bound.
No kernel may reach another device: no remote copies, remote signals or barrier semaphores. Data moves between devices by JAX's collectives and lax.ppermute only.
A program may use at most 128 MiB of HBM per device.

```python
import math
import jax
import jax.numpy as jnp
import numpy as np
from jax import lax

D = 4096
QH = 32
KVH = 8
HD = 128
HID = 7168
EXPERTS = 8
TOP = 2
BLK = 128
TOK_DEV = 128
GROUPS = 16
LEN = 2048
NBLK = 16
DOCS = 4
DOC_MOST = 8
CAP = 40
N_SEQ = 16


def draw_query_rows(key, part):
    base = jnp.clip(jax.random.normal(jax.random.fold_in(key, 1), (GROUPS, LEN, D), jnp.float32), -6.0, 6.0)
    return base.astype(jnp.bfloat16)


def draw_key_rows(key, part):
    base = jnp.clip(jax.random.normal(jax.random.fold_in(key, 2), (GROUPS, LEN, KVH * HD), jnp.float32), -6.0, 6.0)
    return base.astype(jnp.bfloat16)


def draw_value_rows(key, part):
    column_scale = jnp.exp(jax.random.uniform(jax.random.fold_in(key, 31), (KVH * HD,), jnp.float32, math.log(0.3), math.log(3.0)))
    row_scale = jnp.exp(jax.random.uniform(jax.random.fold_in(key, 32), (GROUPS, LEN, 1), jnp.float32, math.log(0.3), math.log(3.0)))
    base = jnp.clip(jax.random.normal(jax.random.fold_in(key, 34), (GROUPS, LEN, KVH * HD), jnp.float32), -3.0, 3.0)
    return (base * column_scale * row_scale).astype(jnp.bfloat16)


def draw_expert_ids(key, part):
    nblocks = GROUPS * LEN // TOK_DEV
    counts = jax.random.randint(jax.random.fold_in(key, 41), (nblocks,), CAP // 3, CAP + 1)
    fullest = jax.random.randint(jax.random.fold_in(key, 42), (), 0, nblocks)
    counts = jnp.where(jnp.arange(nblocks) == fullest, CAP, counts)
    perm_keys = jax.random.split(jax.random.fold_in(key, 43), nblocks)
    perms = jax.vmap(lambda sub: jax.random.permutation(sub, TOK_DEV))(perm_keys)
    routed = perms < counts[:, None]
    which = jax.random.randint(jax.random.fold_in(key, 44), (nblocks, TOK_DEV), 0, 2)
    first = jax.random.randint(jax.random.fold_in(key, 45), (nblocks, TOK_DEV), 1, EXPERTS)
    offset = jax.random.randint(jax.random.fold_in(key, 46), (nblocks, TOK_DEV), 1, EXPERTS - 1)
    second = 1 + (first - 1 + offset) % (EXPERTS - 1)
    id_first = jnp.where(routed & (which == 0), 0, first)
    id_second = jnp.where(routed & (which == 1), 0, second)
    return jnp.stack([id_first, id_second], axis=-1).reshape(GROUPS, LEN, TOP).astype(jnp.int32)


def block_scale(key, shape, cuts, low, top_value):
    loudness = 1.0
    for axis_at, shards_of in cuts:
        draws = jax.random.uniform(jax.random.fold_in(jax.random.fold_in(key, 6), axis_at), (shards_of,), jnp.float32, low / len(cuts), top_value / len(cuts))
        loudness = loudness * jnp.repeat(jnp.exp(draws), shape[axis_at] // shards_of).reshape((-1,) + (1,) * (len(shape) - 1 - axis_at))
    return loudness


def length_profile(number_of, total, reach, slope):
    portions = [(1 << 20) // math.isqrt(grade ** slope) + 1 for grade in range(2, number_of + 1)]
    spare, holding = total - reach - (number_of - 1), [1] * (number_of - 1)
    while spare > 0:
        candidates = [i for i in range(number_of - 1) if holding[i] < reach]
        whole, left = sum([portions[i] for i in candidates]), spare
        for i in candidates:
            more = min(reach - holding[i], max(1, left * portions[i] // whole), spare)
            holding[i] = holding[i] + more
            spare = spare - more
    return np.array([reach] + holding)


def ragged(key, count, total, limit, skew):
    if count == 2:
        one = jax.random.randint(key, (), max(1, total - limit), min(limit, total - 1) + 1)
        return jnp.stack([one, total - one])
    tallies = jnp.asarray(length_profile(count, total, limit, skew), jnp.int32)
    pairs = (count - 1) // 2
    donor, sink = tallies[1:1 + 2 * pairs:2], tallies[2:2 + 2 * pairs:2]
    slack = jnp.minimum(donor - 1, limit - sink)
    shifted = jax.random.randint(jax.random.fold_in(key, 1), (pairs,), 0, 1 << 20) % (slack + 1)
    tallies = tallies.at[1:1 + 2 * pairs:2].set(donor - shifted).at[2:2 + 2 * pairs:2].set(sink + shifted)
    return tallies[jax.random.permutation(jax.random.fold_in(key, 2), count)]


def noise(rng, extent, width, reach, cuts=(), kind=jnp.bfloat16):
    values = jax.random.normal(rng, extent, jnp.float32) * width
    if len(cuts) > 0:
        values = block_scale(rng, extent, cuts, -0.22, 0.18) * values
    return jnp.clip(values, min=-reach, max=reach).astype(kind)


def setup_inputs(seed: int = 0) -> dict:
    keys = jax.random.split(jax.random.key(seed), 10)
    return {
        "query_rows": draw_query_rows(jax.random.fold_in(keys[9], 71), 0),
        "key_rows": draw_key_rows(jax.random.fold_in(keys[9], 71), 0),
        "value_rows": draw_value_rows(jax.random.fold_in(keys[9], 71), 0),
        "doc_of_block": jax.vmap(lambda own: jnp.searchsorted(jnp.cumsum(ragged(own, DOCS, NBLK, DOC_MOST, 2)), jnp.arange(NBLK), side="right"))(jax.random.split(keys[3], GROUPS)).reshape((GROUPS, NBLK)).astype(jnp.int32),
        "expert_ids": draw_expert_ids(jax.random.fold_in(keys[9], 71), 0),
        "gate_weights": jnp.clip(0.1 + 0.79999997 * jax.random.uniform(keys[5], (GROUPS, LEN, TOP), jnp.float32) ** block_scale(keys[5], (GROUPS, LEN, TOP), ((0, 16), (1, 16)), -0.2, 0.2), 0.1, 0.9),
        "norm_gain": jnp.clip(1.0 + 0.18 * jax.random.normal(keys[6], (D,), jnp.float32), 0.1, 1.9),
        "w_in": noise(keys[7], (2, HID, D), D ** -0.5, 0.09375, ((1, 256),)),
        "w_down": noise(keys[8], (HID, D), HID ** -0.5, 0.0625, ((0, 256),)),
    }


EPS = 1e-05
NEG = -1e+30

def attend_group(query_group, key_group, value_group, doc_group):
    token_doc = jnp.repeat(doc_group, BLK)
    allowed = token_doc[:, None] == token_doc[None, :]
    query_heads = jnp.transpose(query_group.astype(jnp.float32).reshape(LEN, QH, HD), (1, 0, 2))
    key_heads = jnp.transpose(key_group.astype(jnp.float32).reshape(LEN, KVH, HD), (1, 0, 2))
    value_heads = jnp.transpose(value_group.astype(jnp.float32).reshape(LEN, KVH, HD), (1, 0, 2))

    def one_head(head):
        query_one = query_heads[head]
        key_one = key_heads[head // 4]
        value_one = value_heads[head // 4]
        scores = jnp.dot(query_one, key_one.T, precision=lax.Precision.HIGHEST) * (1.0 / math.sqrt(HD))
        scores = jnp.where(allowed, scores, NEG)
        highest = lax.optimization_barrier(jnp.max(scores, axis=1, keepdims=True))
        weights = jnp.where(allowed, jnp.exp(scores - highest), 0.0)
        denom = lax.optimization_barrier(jnp.sum(weights, axis=1, keepdims=True))
        rounded = lax.optimization_barrier(weights.astype(jnp.bfloat16)).astype(jnp.float32)
        return jnp.dot(rounded, value_one, precision=lax.Precision.HIGHEST) / denom
    mixed = lax.map(one_head, jnp.arange(QH))
    return jnp.transpose(mixed, (1, 0, 2)).reshape(LEN, D).astype(jnp.bfloat16)

def reference(query_rows, key_rows, value_rows, doc_of_block, expert_ids, gate_weights, norm_gain, w_in, w_down):
    attended = lax.map(lambda parts: attend_group(parts[0], parts[1], parts[2], parts[3]), (query_rows, key_rows, value_rows, doc_of_block))
    attn_float = attended.astype(jnp.float32)
    spread = lax.optimization_barrier(jnp.mean(attn_float * attn_float, axis=-1, keepdims=True))
    normed = (attn_float * lax.rsqrt(spread + EPS) * norm_gain).astype(jnp.bfloat16)
    blocks = GROUPS * N_SEQ
    normed_blocks = normed.reshape(blocks, TOK_DEV, D).astype(jnp.float32)
    route_ids = expert_ids.reshape(blocks, TOK_DEV, TOP)
    chosen = route_ids == 0
    routed = jnp.any(chosen, axis=-1)
    gate_share = lax.optimization_barrier(jnp.sum(jnp.where(chosen, gate_weights.reshape(blocks, TOK_DEV, TOP), 0.0), axis=-1))
    slot_index = jnp.cumsum(routed.astype(jnp.int32), axis=1).astype(jnp.int32) - 1
    slot_ids = jnp.arange(CAP, dtype=jnp.int32)
    onehot = ((slot_index[:, None, :] == slot_ids[None, :, None]) & routed[:, None, :]).astype(jnp.float32)
    dispatched = jnp.einsum('bct,btd->bcd', onehot, normed_blocks, precision=lax.Precision.HIGHEST)
    weights_in = w_in.astype(jnp.float32)
    weights_down = w_down.astype(jnp.float32)

    def expert_rows(row_block):
        gate_up = jnp.einsum('rd,khd->krh', row_block, weights_in, precision=lax.Precision.HIGHEST)
        hidden = (jax.nn.silu(gate_up[0]) * gate_up[1]).astype(jnp.bfloat16)
        hidden = lax.optimization_barrier(hidden).astype(jnp.float32)
        return jnp.dot(hidden, weights_down, precision=lax.Precision.HIGHEST)
    results = lax.map(expert_rows, dispatched.reshape(GROUPS, N_SEQ * CAP, D))
    results = results.reshape(blocks, CAP, D)
    expert_out = jnp.einsum('bct,bcd->btd', onehot, results, precision=lax.Precision.HIGHEST)
    layer_out = attn_float.reshape(blocks, TOK_DEV, D) + gate_share[..., None] * expert_out
    return layer_out.reshape(GROUPS, LEN, D).astype(jnp.bfloat16)
```

```python
import math

import jax
import jax.numpy as jnp
from jax import lax
from jax.sharding import PartitionSpec as P


QH = 32
KVH = 8
HD = 128
BLK = 128
CAP = 40


EPS = 1e-05
NEG = -1e30


def attend(query_all, key_all, value_all, token_doc, per_dev):
    seq_length = query_all.shape[0]
    tile_rows = min(512, seq_length)
    tile_count = seq_length // tile_rows
    inv_root = 1.0 / math.sqrt(HD)
    query_split = query_all.reshape(seq_length, per_dev, HD)
    outputs = []
    for q_index in range(tile_count):
        query_tile = query_split[q_index * tile_rows : (q_index + 1) * tile_rows]
        doc_query = token_doc[q_index * tile_rows : (q_index + 1) * tile_rows]
        allowed_row = doc_query[:, None] == token_doc[None, :]
        scores = (
            jnp.einsum("qgd,td->gqt", query_tile, key_all, preferred_element_type=jnp.float32)
            * inv_root
        )
        scores = jnp.where(allowed_row, scores, NEG)
        highest = jnp.max(scores, axis=2, keepdims=True)
        weights = jnp.exp(scores - highest)
        denom = jnp.sum(weights, axis=2, keepdims=True)
        mixed = jnp.einsum(
            "gqt,td->qgd",
            weights.astype(jnp.bfloat16),
            value_all,
            preferred_element_type=jnp.float32,
        )
        mixed = mixed / jnp.transpose(denom, (1, 0, 2))
        outputs.append(mixed.reshape(tile_rows, per_dev * HD).astype(jnp.bfloat16))
    return jnp.concatenate(outputs, axis=0)


def shards_body(
    query_rows,
    key_rows,
    value_rows,
    doc_of_block,
    expert_ids,
    gate_weights,
    norm_gain,
    w_in,
    w_down,
):
    seq_count = lax.axis_size("seq")
    tok_count = query_rows.shape[1]
    per_dev = QH // seq_count
    feat = per_dev * HD
    kv_of_dest = (jnp.arange(seq_count) * per_dev) // (QH // KVH)

    weights_local = jnp.concatenate([w_in, w_down[None]], axis=0)[None]
    weights_all = lax.all_gather(weights_local, "seq", axis=0, tiled=True)

    query_send = jnp.transpose(query_rows[0].reshape(tok_count, seq_count, feat), (1, 0, 2))
    key_send = jnp.transpose(key_rows[0].reshape(tok_count, KVH, HD)[:, kv_of_dest, :], (1, 0, 2))
    value_send = jnp.transpose(
        value_rows[0].reshape(tok_count, KVH, HD)[:, kv_of_dest, :], (1, 0, 2)
    )
    packed = jnp.concatenate([query_send, key_send, value_send], axis=2)
    packed_all = lax.all_to_all(packed, "seq", 0, 0, tiled=False)
    seq_length = seq_count * tok_count
    query_all = packed_all[:, :, :feat].reshape(seq_length, feat)
    key_all = packed_all[:, :, feat : feat + HD].reshape(seq_length, HD)
    value_all = packed_all[:, :, feat + HD :].reshape(seq_length, HD)

    token_doc = jnp.repeat(doc_of_block[0], BLK)
    attended = attend(query_all, key_all, value_all, token_doc, per_dev)
    attn_back = lax.all_to_all(
        attended.reshape(seq_count, tok_count, feat), "seq", 0, 0, tiled=False
    )
    attn_tokens = jnp.transpose(attn_back, (1, 0, 2)).reshape(tok_count, seq_count * feat)
    attn_float = attn_tokens.astype(jnp.float32)
    spread = jnp.mean(attn_float * attn_float, axis=-1, keepdims=True)
    normed = (attn_float * lax.rsqrt(spread + EPS) * norm_gain).astype(jnp.bfloat16)
    chosen = expert_ids[0] == 0
    routed = jnp.any(chosen, axis=-1)
    gate_share = jnp.sum(jnp.where(chosen, gate_weights[0], 0.0), axis=-1)
    slot_index = jnp.cumsum(routed.astype(jnp.int32)) - 1
    onehot = (slot_index[None, :] == jnp.arange(CAP, dtype=jnp.int32)[:, None]) & routed[None, :]
    dispatched = jnp.dot(
        onehot.astype(jnp.bfloat16), normed, preferred_element_type=jnp.float32
    ).astype(jnp.bfloat16)
    gathered = lax.all_gather(dispatched, "grp", axis=0, tiled=True)
    gate_up = jnp.einsum(
        "rd,jkud->krju", gathered, weights_all[:, :2], preferred_element_type=jnp.float32
    )
    hidden = (jax.nn.silu(gate_up[0]) * gate_up[1]).astype(jnp.bfloat16)
    terms = jnp.einsum(
        "rju,jud->rd", hidden, weights_all[:, 2], preferred_element_type=jnp.float32
    )
    returned = lax.psum_scatter(
        terms.astype(jnp.bfloat16), "grp", scatter_dimension=0, tiled=True
    ).astype(jnp.float32)
    picked_rows = jnp.take(returned, jnp.clip(slot_index, 0, CAP - 1), axis=0)
    expert_out = jnp.where(routed[:, None], picked_rows, 0.0)
    layer_out = attn_float + gate_share[:, None] * expert_out
    return layer_out.astype(jnp.bfloat16)[None]


def solution(mesh):
    return jax.shard_map(
        shards_body,
        mesh=mesh,
        in_specs=(
            P("grp", "seq", None),
            P("grp", "seq", None),
            P("grp", "seq", None),
            P("grp", None),
            P("grp", "seq", None),
            P("grp", "seq", None),
            P(),
            P(None, ("seq", "grp"), None),
            P(("seq", "grp"), None),
        ),
        out_specs=P("grp", "seq", None),
        check_vma=False,
    )
```

```python
import math

import jax
import jax.numpy as jnp
from jax import lax
from jax.sharding import PartitionSpec as P


QH = 32
KVH = 8
HD = 128
BLK = 128
CAP = 40


EPS = 1e-05
NEG = -1e30


def attend(query_all, key_all, value_all, token_doc, per_dev):
    seq_length = query_all.shape[0]
    tile_rows = min(512, seq_length)
    tile_count = seq_length // tile_rows
    inv_root = 1.0 / math.sqrt(HD)
    query_split = query_all.reshape(seq_length, per_dev, HD)
    outputs = []
    for q_index in range(tile_count):
        query_tile = query_split[q_index * tile_rows : (q_index + 1) * tile_rows]
        doc_query = token_doc[q_index * tile_rows : (q_index + 1) * tile_rows]
        allowed_row = doc_query[:, None] == token_doc[None, :]
        scores = (
            jnp.einsum("qgd,td->gqt", query_tile, key_all, preferred_element_type=jnp.float32)
            * inv_root
        )
        scores = jnp.where(allowed_row, scores, NEG)
        highest = jnp.max(scores, axis=2, keepdims=True)
        weights = jnp.exp(scores - highest)
        denom = jnp.sum(weights, axis=2, keepdims=True)
        mixed = jnp.einsum(
            "gqt,td->qgd",
            weights.astype(jnp.bfloat16),
            value_all,
            preferred_element_type=jnp.float32,
        )
        mixed = mixed / jnp.transpose(denom, (1, 0, 2))
        outputs.append(mixed.reshape(tile_rows, per_dev * HD).astype(jnp.bfloat16))
    return jnp.concatenate(outputs, axis=0)


def shards_body(
    query_rows,
    key_rows,
    value_rows,
    doc_of_block,
    expert_ids,
    gate_weights,
    norm_gain,
    w_in,
    w_down,
):
    seq_count = lax.axis_size("seq")
    tok_count = query_rows.shape[1]
    per_dev = QH // seq_count
    feat = per_dev * HD
    kv_of_dest = (jnp.arange(seq_count) * per_dev) // (QH // KVH)

    weights_local = jnp.concatenate([w_in, w_down[None]], axis=0)[None]
    weights_all = lax.all_gather(weights_local, "grp", axis=0, tiled=True)

    query_send = jnp.transpose(query_rows[0].reshape(tok_count, seq_count, feat), (1, 0, 2))
    key_send = jnp.transpose(key_rows[0].reshape(tok_count, KVH, HD)[:, kv_of_dest, :], (1, 0, 2))
    value_send = jnp.transpose(
        value_rows[0].reshape(tok_count, KVH, HD)[:, kv_of_dest, :], (1, 0, 2)
    )
    packed = jnp.concatenate([query_send, key_send, value_send], axis=2)
    packed_all = lax.all_to_all(packed, "seq", 0, 0, tiled=False)
    seq_length = seq_count * tok_count
    query_all = packed_all[:, :, :feat].reshape(seq_length, feat)
    key_all = packed_all[:, :, feat : feat + HD].reshape(seq_length, HD)
    value_all = packed_all[:, :, feat + HD :].reshape(seq_length, HD)

    token_doc = jnp.repeat(doc_of_block[0], BLK)
    attended = attend(query_all, key_all, value_all, token_doc, per_dev)
    attn_back = lax.all_to_all(
        attended.reshape(seq_count, tok_count, feat), "seq", 0, 0, tiled=False
    )
    attn_tokens = jnp.transpose(attn_back, (1, 0, 2)).reshape(tok_count, seq_count * feat)
    attn_float = attn_tokens.astype(jnp.float32)
    spread = jnp.mean(attn_float * attn_float, axis=-1, keepdims=True)
    normed = (attn_float * lax.rsqrt(spread + EPS) * norm_gain).astype(jnp.bfloat16)
    chosen = expert_ids[0] == 0
    routed = jnp.any(chosen, axis=-1)
    gate_share = jnp.sum(jnp.where(chosen, gate_weights[0], 0.0), axis=-1)
    slot_index = jnp.cumsum(routed.astype(jnp.int32)) - 1
    onehot = (slot_index[None, :] == jnp.arange(CAP, dtype=jnp.int32)[:, None]) & routed[None, :]
    dispatched = jnp.dot(
        onehot.astype(jnp.bfloat16), normed, preferred_element_type=jnp.float32
    ).astype(jnp.bfloat16)
    gathered = lax.all_gather(dispatched, "seq", axis=0, tiled=True)
    gate_up = jnp.einsum(
        "rd,jkud->krju", gathered, weights_all[:, :2], preferred_element_type=jnp.float32
    )
    hidden = (jax.nn.silu(gate_up[0]) * gate_up[1]).astype(jnp.bfloat16)
    terms = jnp.einsum(
        "rju,jud->rd", hidden, weights_all[:, 2], preferred_element_type=jnp.float32
    )
    returned = lax.psum_scatter(
        terms.astype(jnp.bfloat16), "seq", scatter_dimension=0, tiled=True
    ).astype(jnp.float32)
    picked_rows = jnp.take(returned, jnp.clip(slot_index, 0, CAP - 1), axis=0)
    expert_out = jnp.where(routed[:, None], picked_rows, 0.0)
    layer_out = attn_float + gate_share[:, None] * expert_out
    return layer_out.astype(jnp.bfloat16)[None]


def solution(mesh):
    return jax.shard_map(
        shards_body,
        mesh=mesh,
        in_specs=(
            P("grp", "seq", None),
            P("grp", "seq", None),
            P("grp", "seq", None),
            P("grp", None),
            P("grp", "seq", None),
            P("grp", "seq", None),
            P(),
            P(None, ("seq", "grp"), None),
            P(("seq", "grp"), None),
        ),
        out_specs=P("grp", "seq", None),
        check_vma=False,
    )
```

```python
import math

import jax
import jax.numpy as jnp
from jax import lax
from jax.sharding import PartitionSpec as P


QH = 32
KVH = 8
HD = 128
BLK = 128
CAP = 40


EPS = 1e-05
NEG = -1e30


def attend(query_all, key_all, value_all, token_doc, per_dev):
    seq_length = query_all.shape[0]
    tile_rows = min(512, seq_length)
    tile_count = seq_length // tile_rows
    inv_root = 1.0 / math.sqrt(HD)
    query_split = query_all.reshape(seq_length, per_dev, HD)
    outputs = []
    for q_index in range(tile_count):
        query_tile = query_split[q_index * tile_rows : (q_index + 1) * tile_rows]
        doc_query = token_doc[q_index * tile_rows : (q_index + 1) * tile_rows]
        allowed_row = doc_query[:, None] == token_doc[None, :]
        scores = (
            jnp.einsum("qgd,td->gqt", query_tile, key_all, preferred_element_type=jnp.float32)
            * inv_root
        )
        scores = jnp.where(allowed_row, scores, NEG)
        highest = jnp.max(scores, axis=2, keepdims=True)
        weights = jnp.exp(scores - highest)
        denom = jnp.sum(weights, axis=2, keepdims=True)
        mixed = jnp.einsum(
            "gqt,td->qgd",
            weights.astype(jnp.bfloat16),
            value_all,
            preferred_element_type=jnp.float32,
        )
        mixed = mixed / jnp.transpose(denom, (1, 0, 2))
        outputs.append(mixed.reshape(tile_rows, per_dev * HD).astype(jnp.bfloat16))
    return jnp.concatenate(outputs, axis=0)


def shards_body(
    query_rows,
    key_rows,
    value_rows,
    doc_of_block,
    expert_ids,
    gate_weights,
    norm_gain,
    w_in,
    w_down,
):
    seq_count = lax.axis_size("seq")
    tok_count = query_rows.shape[1]
    per_dev = QH // seq_count
    feat = per_dev * HD
    kv_of_dest = (jnp.arange(seq_count) * per_dev) // (QH // KVH)

    weights_local = jnp.concatenate([w_in, w_down[None]], axis=0)[None]
    weights_all = lax.all_gather(weights_local, "grp", axis=0, tiled=True)

    query_send = jnp.transpose(query_rows[0].reshape(tok_count, seq_count, feat), (1, 0, 2))
    key_send = jnp.transpose(key_rows[0].reshape(tok_count, KVH, HD)[:, kv_of_dest, :], (1, 0, 2))
    value_send = jnp.transpose(
        value_rows[0].reshape(tok_count, KVH, HD)[:, kv_of_dest, :], (1, 0, 2)
    )
    packed = jnp.concatenate([query_send, key_send, value_send], axis=2)
    packed_all = lax.all_to_all(packed, "seq", 0, 0, tiled=False)
    seq_length = seq_count * tok_count
    query_all = packed_all[:, :, :feat].reshape(seq_length, feat)
    key_all = packed_all[:, :, feat : feat + HD].reshape(seq_length, HD)
    value_all = packed_all[:, :, feat + HD :].reshape(seq_length, HD)

    token_doc = jnp.repeat(doc_of_block[0], BLK)
    attended = attend(query_all, key_all, value_all, token_doc, per_dev)
    attn_back = lax.all_to_all(
        attended.reshape(seq_count, tok_count, feat), "seq", 0, 0, tiled=False
    )
    attn_tokens = jnp.transpose(attn_back, (1, 0, 2)).reshape(tok_count, seq_count * feat)
    attn_float = attn_tokens.astype(jnp.float32)
    spread = jnp.mean(attn_float * attn_float, axis=-1, keepdims=True)
    normed = (attn_float * lax.rsqrt(spread + EPS) * norm_gain).astype(jnp.bfloat16)
    chosen = expert_ids[0] == 0
    routed = jnp.any(chosen, axis=-1)
    gate_share = jnp.sum(jnp.where(chosen, gate_weights[0], 0.0), axis=-1)
    slot_index = jnp.cumsum(routed.astype(jnp.int32)) - 1
    onehot = (slot_index[None, :] == jnp.arange(CAP, dtype=jnp.int32)[:, None]) & routed[None, :]
    dispatched = jnp.dot(
        onehot.astype(jnp.bfloat16), normed, preferred_element_type=jnp.float32
    ).astype(jnp.bfloat16)
    gathered = lax.all_gather(dispatched, "seq", axis=0, tiled=True)
    gate_up = jnp.einsum(
        "rd,jkud->krju", gathered, weights_all[:, :2], preferred_element_type=jnp.float32
    )
    hidden = (jax.nn.silu(gate_up[0]) * gate_up[1]).astype(jnp.bfloat16)
    terms = jnp.einsum(
        "rju,jud->rd", hidden, weights_all[:, 2], preferred_element_type=jnp.float32
    )
    partials = lax.all_to_all(
        terms.astype(jnp.bfloat16).reshape(seq_count, CAP, -1), "seq", 0, 0, tiled=False
    )
    returned = jnp.sum(partials.astype(jnp.float32), axis=0)
    picked_rows = jnp.take(returned, jnp.clip(slot_index, 0, CAP - 1), axis=0)
    expert_out = jnp.where(routed[:, None], picked_rows, 0.0)
    layer_out = attn_float + gate_share[:, None] * expert_out
    return layer_out.astype(jnp.bfloat16)[None]


def solution(mesh):
    return jax.shard_map(
        shards_body,
        mesh=mesh,
        in_specs=(
            P("grp", "seq", None),
            P("grp", "seq", None),
            P("grp", "seq", None),
            P("grp", None),
            P("grp", "seq", None),
            P("grp", "seq", None),
            P(),
            P(None, ("seq", "grp"), None),
            P(("seq", "grp"), None),
        ),
        out_specs=P("grp", "seq", None),
        check_vma=False,
    )
```

```python
import math

import jax
import jax.numpy as jnp
from jax import lax
from jax.sharding import PartitionSpec as P


QH = 32
KVH = 8
HD = 128
BLK = 128
CAP = 40


EPS = 1e-05
NEG = -1e30


def attend(query_all, key_all, value_all, token_doc, per_dev):
    seq_length = query_all.shape[0]
    tile_rows = min(512, seq_length)
    tile_count = seq_length // tile_rows
    inv_root = 1.0 / math.sqrt(HD)
    query_split = query_all.reshape(seq_length, per_dev, HD)
    outputs = []
    for q_index in range(tile_count):
        query_tile = query_split[q_index * tile_rows : (q_index + 1) * tile_rows]
        doc_query = token_doc[q_index * tile_rows : (q_index + 1) * tile_rows]
        allowed_row = doc_query[:, None] == token_doc[None, :]
        scores = (
            jnp.einsum("qgd,td->gqt", query_tile, key_all, preferred_element_type=jnp.float32)
            * inv_root
        )
        scores = jnp.where(allowed_row, scores, NEG)
        highest = jnp.max(scores, axis=2, keepdims=True)
        weights = jnp.exp(scores - highest)
        denom = jnp.sum(weights, axis=2, keepdims=True)
        mixed = jnp.einsum(
            "gqt,td->qgd",
            weights.astype(jnp.bfloat16),
            value_all,
            preferred_element_type=jnp.float32,
        )
        mixed = mixed / jnp.transpose(denom, (1, 0, 2))
        outputs.append(mixed.reshape(tile_rows, per_dev * HD).astype(jnp.bfloat16))
    return jnp.concatenate(outputs, axis=0)


def shards_body(
    query_rows,
    key_rows,
    value_rows,
    doc_of_block,
    expert_ids,
    gate_weights,
    norm_gain,
    w_in,
    w_down,
):
    seq_count = lax.axis_size("seq")
    tok_count = query_rows.shape[1]
    per_dev = QH // seq_count
    feat = per_dev * HD
    kv_of_dest = (jnp.arange(seq_count) * per_dev) // (QH // KVH)

    weights_local = jnp.concatenate([w_in, w_down[None]], axis=0)[None]
    weights_all = lax.all_gather(weights_local, "seq", axis=0, tiled=True)

    query_send = jnp.transpose(query_rows[0].reshape(tok_count, seq_count, feat), (1, 0, 2))
    key_send = jnp.transpose(key_rows[0].reshape(tok_count, KVH, HD)[:, kv_of_dest, :], (1, 0, 2))
    value_send = jnp.transpose(
        value_rows[0].reshape(tok_count, KVH, HD)[:, kv_of_dest, :], (1, 0, 2)
    )
    packed = jnp.concatenate([query_send, key_send, value_send], axis=2)
    packed_all = lax.all_to_all(packed, "seq", 0, 0, tiled=False)
    seq_length = seq_count * tok_count
    query_all = packed_all[:, :, :feat].reshape(seq_length, feat)
    key_all = packed_all[:, :, feat : feat + HD].reshape(seq_length, HD)
    value_all = packed_all[:, :, feat + HD :].reshape(seq_length, HD)

    token_doc = jnp.repeat(doc_of_block[0], BLK)
    attended = attend(query_all, key_all, value_all, token_doc, per_dev)
    attn_back = lax.all_to_all(
        attended.reshape(seq_count, tok_count, feat), "seq", 0, 0, tiled=False
    )
    attn_tokens = jnp.transpose(attn_back, (1, 0, 2)).reshape(tok_count, seq_count * feat)
    attn_float = attn_tokens.astype(jnp.float32)
    spread = jnp.mean(attn_float * attn_float, axis=-1, keepdims=True)
    normed = (attn_float * lax.rsqrt(spread + EPS) * norm_gain).astype(jnp.bfloat16)
    chosen = expert_ids[0] == 0
    routed = jnp.any(chosen, axis=-1)
    gate_share = jnp.sum(jnp.where(chosen, gate_weights[0], 0.0), axis=-1)
    slot_index = jnp.cumsum(routed.astype(jnp.int32)) - 1
    onehot = (slot_index[None, :] == jnp.arange(CAP, dtype=jnp.int32)[:, None]) & routed[None, :]
    dispatched = jnp.dot(
        onehot.astype(jnp.bfloat16), normed, preferred_element_type=jnp.float32
    ).astype(jnp.bfloat16)
    gathered = lax.all_gather(dispatched, "grp", axis=0, tiled=True)
    grp_count = gathered.shape[0] // CAP
    by_source = gathered.reshape(grp_count, CAP, -1)
    cuts = (0, 24, CAP)
    pieces = []
    for part in range(2):
        lo, hi = cuts[part], cuts[part + 1]
        rows = by_source[:, lo:hi].reshape(grp_count * (hi - lo), -1)
        gate_up = jnp.einsum(
            "rd,jkud->krju", rows, weights_all[:, :2], preferred_element_type=jnp.float32
        )
        hidden = (jax.nn.silu(gate_up[0]) * gate_up[1]).astype(jnp.bfloat16)
        terms = jnp.einsum(
            "rju,jud->rd", hidden, weights_all[:, 2], preferred_element_type=jnp.float32
        )
        pieces.append(
            lax.psum_scatter(
                terms.astype(jnp.bfloat16), "grp", scatter_dimension=0, tiled=True
            )
        )
    returned = jnp.concatenate(pieces, axis=0).astype(jnp.float32)
    picked_rows = jnp.take(returned, jnp.clip(slot_index, 0, CAP - 1), axis=0)
    expert_out = jnp.where(routed[:, None], picked_rows, 0.0)
    layer_out = attn_float + gate_share[:, None] * expert_out
    return layer_out.astype(jnp.bfloat16)[None]


def solution(mesh):
    return jax.shard_map(
        shards_body,
        mesh=mesh,
        in_specs=(
            P("grp", "seq", None),
            P("grp", "seq", None),
            P("grp", "seq", None),
            P("grp", None),
            P("grp", "seq", None),
            P("grp", "seq", None),
            P(),
            P(None, ("seq", "grp"), None),
            P(("seq", "grp"), None),
        ),
        out_specs=P("grp", "seq", None),
        check_vma=False,
    )
```

```python
import math

import jax
import jax.numpy as jnp
from jax import lax
from jax.sharding import PartitionSpec as P


QH = 32
KVH = 8
HD = 128
BLK = 128
CAP = 40


EPS = 1e-05
NEG = -1e30


def attend(query_all, key_all, value_all, token_doc, per_dev):
    seq_length = query_all.shape[0]
    tile_rows = min(512, seq_length)
    tile_count = seq_length // tile_rows
    inv_root = 1.0 / math.sqrt(HD)
    query_split = query_all.reshape(seq_length, per_dev, HD)
    outputs = []
    for q_index in range(tile_count):
        query_tile = query_split[q_index * tile_rows : (q_index + 1) * tile_rows]
        doc_query = token_doc[q_index * tile_rows : (q_index + 1) * tile_rows]
        allowed_row = doc_query[:, None] == token_doc[None, :]
        scores = (
            jnp.einsum("qgd,td->gqt", query_tile, key_all, preferred_element_type=jnp.float32)
            * inv_root
        )
        scores = jnp.where(allowed_row, scores, NEG)
        highest = jnp.max(scores, axis=2, keepdims=True)
        weights = jnp.exp(scores - highest)
        denom = jnp.sum(weights, axis=2, keepdims=True)
        mixed = jnp.einsum(
            "gqt,td->qgd",
            weights.astype(jnp.bfloat16),
            value_all,
            preferred_element_type=jnp.float32,
        )
        mixed = mixed / jnp.transpose(denom, (1, 0, 2))
        outputs.append(mixed.reshape(tile_rows, per_dev * HD).astype(jnp.bfloat16))
    return jnp.concatenate(outputs, axis=0)


def shards_body(
    query_rows,
    key_rows,
    value_rows,
    doc_of_block,
    expert_ids,
    gate_weights,
    norm_gain,
    w_in,
    w_down,
):
    seq_count = lax.axis_size("seq")
    tok_count = query_rows.shape[1]
    per_dev = QH // seq_count
    feat = per_dev * HD
    kv_of_dest = (jnp.arange(seq_count) * per_dev) // (QH // KVH)

    weights_local = jnp.concatenate([w_in, w_down[None]], axis=0).reshape(-1)
    weights_flat = lax.all_gather(weights_local, "seq", axis=0, tiled=True)
    weights_all = weights_flat.reshape((seq_count,) + (3,) + w_down.shape)

    query_send = jnp.transpose(query_rows[0].reshape(tok_count, seq_count, feat), (1, 0, 2))
    key_send = jnp.transpose(key_rows[0].reshape(tok_count, KVH, HD)[:, kv_of_dest, :], (1, 0, 2))
    value_send = jnp.transpose(
        value_rows[0].reshape(tok_count, KVH, HD)[:, kv_of_dest, :], (1, 0, 2)
    )
    packed = jnp.concatenate([query_send, key_send, value_send], axis=2)
    packed_all = lax.all_to_all(packed, "seq", 0, 0, tiled=False)
    seq_length = seq_count * tok_count
    query_all = packed_all[:, :, :feat].reshape(seq_length, feat)
    key_all = packed_all[:, :, feat : feat + HD].reshape(seq_length, HD)
    value_all = packed_all[:, :, feat + HD :].reshape(seq_length, HD)

    token_doc = jnp.repeat(doc_of_block[0], BLK)
    attended = attend(query_all, key_all, value_all, token_doc, per_dev)
    attn_back = lax.all_to_all(
        attended.reshape(seq_count, tok_count, feat), "seq", 0, 0, tiled=False
    )
    attn_tokens = jnp.transpose(attn_back, (1, 0, 2)).reshape(tok_count, seq_count * feat)
    attn_float = attn_tokens.astype(jnp.float32)
    spread = jnp.mean(attn_float * attn_float, axis=-1, keepdims=True)
    normed = (attn_float * lax.rsqrt(spread + EPS) * norm_gain).astype(jnp.bfloat16)
    chosen = expert_ids[0] == 0
    routed = jnp.any(chosen, axis=-1)
    gate_share = jnp.sum(jnp.where(chosen, gate_weights[0], 0.0), axis=-1)
    slot_index = jnp.cumsum(routed.astype(jnp.int32)) - 1
    onehot = (slot_index[None, :] == jnp.arange(CAP, dtype=jnp.int32)[:, None]) & routed[None, :]
    dispatched = jnp.dot(
        onehot.astype(jnp.bfloat16), normed, preferred_element_type=jnp.float32
    ).astype(jnp.bfloat16)
    gathered = lax.all_gather(dispatched, "grp", axis=0, tiled=True)
    gate_up = jnp.einsum(
        "rd,jkud->krju", gathered, weights_all[:, :2], preferred_element_type=jnp.float32
    )
    hidden = (jax.nn.silu(gate_up[0]) * gate_up[1]).astype(jnp.bfloat16)
    terms = jnp.einsum(
        "rju,jud->rd", hidden, weights_all[:, 2], preferred_element_type=jnp.float32
    )
    returned = lax.psum_scatter(
        terms.astype(jnp.bfloat16), "grp", scatter_dimension=0, tiled=True
    ).astype(jnp.float32)
    picked_rows = jnp.take(returned, jnp.clip(slot_index, 0, CAP - 1), axis=0)
    expert_out = jnp.where(routed[:, None], picked_rows, 0.0)
    layer_out = attn_float + gate_share[:, None] * expert_out
    return layer_out.astype(jnp.bfloat16)[None]


def solution(mesh):
    return jax.shard_map(
        shards_body,
        mesh=mesh,
        in_specs=(
            P("grp", "seq", None),
            P("grp", "seq", None),
            P("grp", "seq", None),
            P("grp", None),
            P("grp", "seq", None),
            P("grp", "seq", None),
            P(),
            P(None, ("seq", "grp"), None),
            P(("seq", "grp"), None),
        ),
        out_specs=P("grp", "seq", None),
        check_vma=False,
    )
```

```python
import math

import jax
import jax.numpy as jnp
from jax import lax
from jax.sharding import PartitionSpec as P


QH = 32
KVH = 8
HD = 128
BLK = 128
CAP = 40


EPS = 1e-05
NEG = -1e30


def attend(query_all, key_all, value_all, token_doc, per_dev):
    seq_length = query_all.shape[0]
    tile_rows = min(512, seq_length)
    tile_count = seq_length // tile_rows
    inv_root = 1.0 / math.sqrt(HD)
    query_split = query_all.reshape(seq_length, per_dev, HD)
    outputs = []
    for q_index in range(tile_count):
        query_tile = query_split[q_index * tile_rows : (q_index + 1) * tile_rows]
        doc_query = token_doc[q_index * tile_rows : (q_index + 1) * tile_rows]
        allowed_row = doc_query[:, None] == token_doc[None, :]
        scores = (
            jnp.einsum("qgd,td->gqt", query_tile, key_all, preferred_element_type=jnp.float32)
            * inv_root
        )
        scores = jnp.where(allowed_row, scores, NEG)
        highest = jnp.max(scores, axis=2, keepdims=True)
        weights = jnp.exp(scores - highest)
        denom = jnp.sum(weights, axis=2, keepdims=True)
        mixed = jnp.einsum(
            "gqt,td->qgd",
            weights.astype(jnp.bfloat16),
            value_all,
            preferred_element_type=jnp.float32,
        )
        mixed = mixed / jnp.transpose(denom, (1, 0, 2))
        outputs.append(mixed.reshape(tile_rows, per_dev * HD).astype(jnp.bfloat16))
    return jnp.concatenate(outputs, axis=0)


def shards_body(
    query_rows,
    key_rows,
    value_rows,
    doc_of_block,
    expert_ids,
    gate_weights,
    norm_gain,
    w_in,
    w_down,
):
    seq_count = lax.axis_size("seq")
    tok_count = query_rows.shape[1]
    per_dev = QH // seq_count
    feat = per_dev * HD

    weights_local = jnp.concatenate(
        [jnp.transpose(w_in, (1, 0, 2)).reshape(-1), w_down.reshape(-1)]
    )
    weights_flat = lax.all_gather(weights_local, "seq", axis=0, tiled=True)
    per_source = weights_flat.reshape(seq_count, -1)
    in_size = w_in.size
    w_in_all = per_source[:, :in_size].reshape(seq_count, w_in.shape[1], 2, w_in.shape[2])
    w_down_all = per_source[:, in_size:].reshape((seq_count,) + w_down.shape)

    query_send = jnp.transpose(query_rows[0].reshape(tok_count, seq_count, feat), (1, 0, 2))
    kv_repeat = seq_count // KVH
    key_send = jnp.repeat(
        jnp.transpose(key_rows[0].reshape(tok_count, KVH, HD), (1, 0, 2)), kv_repeat, axis=0
    )
    value_send = jnp.repeat(
        jnp.transpose(value_rows[0].reshape(tok_count, KVH, HD), (1, 0, 2)), kv_repeat, axis=0
    )
    packed = jnp.concatenate([query_send, key_send, value_send], axis=2)
    packed_all = lax.all_to_all(packed, "seq", 0, 0, tiled=False)
    seq_length = seq_count * tok_count
    query_all = packed_all[:, :, :feat].reshape(seq_length, feat)
    key_all = packed_all[:, :, feat : feat + HD].reshape(seq_length, HD)
    value_all = packed_all[:, :, feat + HD :].reshape(seq_length, HD)

    token_doc = jnp.repeat(doc_of_block[0], BLK)
    attended = attend(query_all, key_all, value_all, token_doc, per_dev)
    attn_back = lax.all_to_all(
        attended.reshape(seq_count, tok_count, feat), "seq", 0, 0, tiled=False
    )
    attn_tokens = jnp.transpose(attn_back, (1, 0, 2)).reshape(tok_count, seq_count * feat)
    attn_float = attn_tokens.astype(jnp.float32)
    spread = jnp.mean(attn_float * attn_float, axis=-1, keepdims=True)
    normed = (attn_float * lax.rsqrt(spread + EPS) * norm_gain).astype(jnp.bfloat16)
    chosen = expert_ids[0] == 0
    routed = jnp.any(chosen, axis=-1)
    gate_share = jnp.sum(jnp.where(chosen, gate_weights[0], 0.0), axis=-1)
    slot_index = jnp.cumsum(routed.astype(jnp.int32)) - 1
    onehot = (slot_index[None, :] == jnp.arange(CAP, dtype=jnp.int32)[:, None]) & routed[None, :]
    dispatched = jnp.dot(
        onehot.astype(jnp.bfloat16), normed, preferred_element_type=jnp.float32
    ).astype(jnp.bfloat16)
    gathered = lax.all_gather(dispatched, "grp", axis=0, tiled=True)
    gate_up = jnp.einsum(
        "rd,jukd->krju", gathered, w_in_all, preferred_element_type=jnp.float32
    )
    hidden = (jax.nn.silu(gate_up[0]) * gate_up[1]).astype(jnp.bfloat16)
    terms = jnp.einsum(
        "rju,jud->rd", hidden, w_down_all, preferred_element_type=jnp.float32
    )
    returned = lax.psum_scatter(
        terms.astype(jnp.bfloat16), "grp", scatter_dimension=0, tiled=True
    ).astype(jnp.float32)
    picked_rows = jnp.take(returned, jnp.clip(slot_index, 0, CAP - 1), axis=0)
    expert_out = jnp.where(routed[:, None], picked_rows, 0.0)
    layer_out = attn_float + gate_share[:, None] * expert_out
    return layer_out.astype(jnp.bfloat16)[None]


def solution(mesh):
    return jax.shard_map(
        shards_body,
        mesh=mesh,
        in_specs=(
            P("grp", "seq", None),
            P("grp", "seq", None),
            P("grp", "seq", None),
            P("grp", None),
            P("grp", "seq", None),
            P("grp", "seq", None),
            P(),
            P(None, ("seq", "grp"), None),
            P(("seq", "grp"), None),
        ),
        out_specs=P("grp", "seq", None),
        check_vma=False,
    )
```

```python
import math

import jax
import jax.numpy as jnp
from jax import lax
from jax.sharding import PartitionSpec as P


QH = 32
KVH = 8
HD = 128
BLK = 128
CAP = 40


EPS = 1e-05
NEG = -1e30


def attend(query_all, key_all, value_all, token_doc, per_dev):
    seq_length = query_all.shape[0]
    tile_rows = min(512, seq_length)
    tile_count = seq_length // tile_rows
    inv_root = 1.0 / math.sqrt(HD)
    query_split = query_all.reshape(seq_length, per_dev, HD)
    outputs = []
    for q_index in range(tile_count):
        query_tile = query_split[q_index * tile_rows : (q_index + 1) * tile_rows]
        doc_query = token_doc[q_index * tile_rows : (q_index + 1) * tile_rows]
        allowed_row = doc_query[:, None] == token_doc[None, :]
        scores = (
            jnp.einsum("qgd,td->gqt", query_tile, key_all, preferred_element_type=jnp.float32)
            * inv_root
        )
        scores = jnp.where(allowed_row, scores, NEG)
        highest = jnp.max(scores, axis=2, keepdims=True)
        weights = jnp.exp(scores - highest)
        denom = jnp.sum(weights, axis=2, keepdims=True)
        mixed = jnp.einsum(
            "gqt,td->qgd",
            weights.astype(jnp.bfloat16),
            value_all,
            preferred_element_type=jnp.float32,
        )
        mixed = mixed / jnp.transpose(denom, (1, 0, 2))
        outputs.append(mixed.reshape(tile_rows, per_dev * HD).astype(jnp.bfloat16))
    return jnp.concatenate(outputs, axis=0)


def shards_body(
    query_rows,
    key_rows,
    value_rows,
    doc_of_block,
    expert_ids,
    gate_weights,
    norm_gain,
    w_in,
    w_down,
):
    seq_count = lax.axis_size("seq")
    tok_count = query_rows.shape[1]
    per_dev = QH // seq_count
    feat = per_dev * HD

    weights_local = jnp.concatenate([w_in, w_down[None]], axis=0).reshape(-1)
    weights_flat = lax.all_gather(weights_local, "seq", axis=0, tiled=True)
    weights_all = weights_flat.reshape((seq_count,) + (3,) + w_down.shape)

    query_send = jnp.transpose(query_rows[0].reshape(tok_count, seq_count, feat), (1, 0, 2))
    kv_repeat = seq_count // KVH
    key_send = jnp.repeat(
        jnp.transpose(key_rows[0].reshape(tok_count, KVH, HD), (1, 0, 2)), kv_repeat, axis=0
    )
    value_send = jnp.repeat(
        jnp.transpose(value_rows[0].reshape(tok_count, KVH, HD), (1, 0, 2)), kv_repeat, axis=0
    )
    packed = jnp.concatenate([query_send, key_send, value_send], axis=2)
    packed_all = lax.all_to_all(packed, "seq", 0, 0, tiled=False)
    seq_length = seq_count * tok_count
    query_all = packed_all[:, :, :feat].reshape(seq_length, feat)
    key_all = packed_all[:, :, feat : feat + HD].reshape(seq_length, HD)
    value_all = packed_all[:, :, feat + HD :].reshape(seq_length, HD)

    token_doc = jnp.repeat(doc_of_block[0], BLK)
    attended = attend(query_all, key_all, value_all, token_doc, per_dev)
    attn_back = lax.all_to_all(
        attended.reshape(seq_count, tok_count, feat), "seq", 0, 0, tiled=False
    )
    attn_tokens = jnp.transpose(attn_back, (1, 0, 2)).reshape(tok_count, seq_count * feat)
    attn_float = attn_tokens.astype(jnp.float32)
    spread = jnp.mean(attn_float * attn_float, axis=-1, keepdims=True)
    normed = (attn_float * lax.rsqrt(spread + EPS) * norm_gain).astype(jnp.bfloat16)
    chosen = expert_ids[0] == 0
    routed = jnp.any(chosen, axis=-1)
    gate_share = jnp.sum(jnp.where(chosen, gate_weights[0], 0.0), axis=-1)
    slot_index = jnp.cumsum(routed.astype(jnp.int32)) - 1
    onehot = (slot_index[None, :] == jnp.arange(CAP, dtype=jnp.int32)[:, None]) & routed[None, :]
    dispatched = jnp.dot(
        onehot.astype(jnp.bfloat16), normed, preferred_element_type=jnp.float32
    ).astype(jnp.bfloat16)
    gathered = lax.all_gather(dispatched, "grp", axis=0, tiled=True)
    gate_up = jnp.einsum(
        "rd,jkud->krju", gathered, weights_all[:, :2], preferred_element_type=jnp.float32
    )
    hidden = (jax.nn.silu(gate_up[0]) * gate_up[1]).astype(jnp.bfloat16)
    terms = jnp.einsum(
        "rju,jud->rd", hidden, weights_all[:, 2], preferred_element_type=jnp.float32
    )
    returned = lax.psum_scatter(
        terms.astype(jnp.bfloat16), "grp", scatter_dimension=0, tiled=True
    ).astype(jnp.float32)
    picked_rows = jnp.take(returned, jnp.clip(slot_index, 0, CAP - 1), axis=0)
    expert_out = jnp.where(routed[:, None], picked_rows, 0.0)
    layer_out = attn_float + gate_share[:, None] * expert_out
    return layer_out.astype(jnp.bfloat16)[None]


def solution(mesh):
    return jax.shard_map(
        shards_body,
        mesh=mesh,
        in_specs=(
            P("grp", "seq", None),
            P("grp", "seq", None),
            P("grp", "seq", None),
            P("grp", None),
            P("grp", "seq", None),
            P("grp", "seq", None),
            P(),
            P(None, ("seq", "grp"), None),
            P(("seq", "grp"), None),
        ),
        out_specs=P("grp", "seq", None),
        check_vma=False,
    )
```

```python
import math

import jax
import jax.numpy as jnp
from jax import lax
from jax.sharding import PartitionSpec as P


QH = 32
KVH = 8
HD = 128
BLK = 128
CAP = 40


EPS = 1e-05
NEG = -1e30


def attend(query_all, key_all, value_all, token_doc, per_dev):
    seq_length = query_all.shape[0]
    tile_rows = min(512, seq_length)
    tile_count = seq_length // tile_rows
    inv_root = 1.0 / math.sqrt(HD)
    query_split = query_all.reshape(seq_length, per_dev, HD)
    outputs = []
    for q_index in range(tile_count):
        query_tile = query_split[q_index * tile_rows : (q_index + 1) * tile_rows]
        doc_query = token_doc[q_index * tile_rows : (q_index + 1) * tile_rows]
        allowed_row = doc_query[:, None] == token_doc[None, :]
        scores = (
            jnp.einsum("qgd,td->gqt", query_tile, key_all, preferred_element_type=jnp.float32)
            * inv_root
        )
        scores = jnp.where(allowed_row, scores, NEG)
        highest = jnp.max(scores, axis=2, keepdims=True)
        weights = jnp.exp(scores - highest)
        denom = jnp.sum(weights, axis=2, keepdims=True)
        mixed = jnp.einsum(
            "gqt,td->qgd",
            weights.astype(jnp.bfloat16),
            value_all,
            preferred_element_type=jnp.float32,
        )
        mixed = mixed / jnp.transpose(denom, (1, 0, 2))
        outputs.append(mixed.reshape(tile_rows, per_dev * HD).astype(jnp.bfloat16))
    return jnp.concatenate(outputs, axis=0)


def shards_body(
    query_rows,
    key_rows,
    value_rows,
    doc_of_block,
    expert_ids,
    gate_weights,
    norm_gain,
    w_in,
    w_down,
):
    seq_count = lax.axis_size("seq")
    tok_count = query_rows.shape[1]
    per_dev = QH // seq_count
    feat = per_dev * HD

    weights_local = jnp.concatenate([w_in, w_down[None]], axis=0).reshape(-1)
    weights_flat = lax.all_gather(weights_local, "seq", axis=0, tiled=True)
    weights_all = weights_flat.reshape((seq_count,) + (3,) + w_down.shape)

    query_send = jnp.transpose(query_rows[0].reshape(tok_count, seq_count, feat), (1, 0, 2))
    kv_repeat = seq_count // KVH
    key_send = jnp.repeat(
        jnp.transpose(key_rows[0].reshape(tok_count, KVH, HD), (1, 0, 2)), kv_repeat, axis=0
    )
    value_send = jnp.repeat(
        jnp.transpose(value_rows[0].reshape(tok_count, KVH, HD), (1, 0, 2)), kv_repeat, axis=0
    )
    packed = jnp.concatenate([query_send, key_send, value_send], axis=2)
    packed_all = lax.all_to_all(packed, "seq", 0, 0, tiled=False)
    seq_length = seq_count * tok_count
    query_all = packed_all[:, :, :feat].reshape(seq_length, feat)
    key_all = packed_all[:, :, feat : feat + HD].reshape(seq_length, HD)
    value_all = packed_all[:, :, feat + HD :].reshape(seq_length, HD)

    token_doc = jnp.repeat(doc_of_block[0], BLK)
    attended = attend(query_all, key_all, value_all, token_doc, per_dev)
    attn_back = lax.all_to_all(
        attended.reshape(seq_count, tok_count, feat), "seq", 0, 0, tiled=False
    )
    attn_tokens = jnp.transpose(attn_back, (1, 0, 2)).reshape(tok_count, seq_count * feat)
    attn_float = attn_tokens.astype(jnp.float32)
    spread = jnp.mean(attn_float * attn_float, axis=-1, keepdims=True)
    normed = (attn_float * lax.rsqrt(spread + EPS) * norm_gain).astype(jnp.bfloat16)
    chosen = expert_ids[0] == 0
    routed = jnp.any(chosen, axis=-1)
    gate_share = jnp.sum(jnp.where(chosen, gate_weights[0], 0.0), axis=-1)
    slot_index = jnp.cumsum(routed.astype(jnp.int32)) - 1
    onehot = (slot_index[None, :] == jnp.arange(CAP, dtype=jnp.int32)[:, None]) & routed[None, :]
    dispatched = jnp.dot(
        onehot.astype(jnp.bfloat16), normed, preferred_element_type=jnp.float32
    ).astype(jnp.bfloat16)
    gathered = lax.all_gather(dispatched, "grp", axis=0, tiled=True)
    gate_up = jnp.einsum(
        "rd,jkud->krju", gathered, weights_all[:, :2], preferred_element_type=jnp.float32
    )
    hidden = (jax.nn.silu(gate_up[0]) * gate_up[1]).astype(jnp.bfloat16)
    terms = jnp.einsum(
        "rju,jud->rd", hidden, weights_all[:, 2], preferred_element_type=jnp.float32
    )
    returned = lax.psum_scatter(
        terms.astype(jnp.bfloat16), "grp", scatter_dimension=0, tiled=True
    )
    expert_out = jnp.dot(
        jnp.transpose(onehot).astype(jnp.bfloat16), returned, preferred_element_type=jnp.float32
    )
    layer_out = attn_float + gate_share[:, None] * expert_out
    return layer_out.astype(jnp.bfloat16)[None]


def solution(mesh):
    return jax.shard_map(
        shards_body,
        mesh=mesh,
        in_specs=(
            P("grp", "seq", None),
            P("grp", "seq", None),
            P("grp", "seq", None),
            P("grp", None),
            P("grp", "seq", None),
            P("grp", "seq", None),
            P(),
            P(None, ("seq", "grp"), None),
            P(("seq", "grp"), None),
        ),
        out_specs=P("grp", "seq", None),
        check_vma=False,
    )
```

```python
import math

import jax
import jax.numpy as jnp
from jax import lax
from jax.sharding import PartitionSpec as P


QH = 32
KVH = 8
HD = 128
BLK = 128
CAP = 40


EPS = 1e-05
NEG = -1e30


def attend(query_all, key_all, value_all, token_doc, per_dev):
    seq_length = query_all.shape[0]
    tile_rows = min(512, seq_length)
    tile_count = seq_length // tile_rows
    inv_root = 1.0 / math.sqrt(HD)
    query_split = query_all.reshape(seq_length, per_dev, HD)
    outputs = []
    for q_index in range(tile_count):
        query_tile = query_split[q_index * tile_rows : (q_index + 1) * tile_rows]
        doc_query = token_doc[q_index * tile_rows : (q_index + 1) * tile_rows]
        allowed_row = doc_query[:, None] == token_doc[None, :]
        scores = (
            jnp.einsum("qgd,td->gqt", query_tile, key_all, preferred_element_type=jnp.float32)
            * inv_root
        )
        scores = jnp.where(allowed_row, scores, NEG)
        highest = jnp.max(scores, axis=2, keepdims=True)
        weights = jnp.exp(scores - highest)
        denom = jnp.sum(weights, axis=2, keepdims=True)
        mixed = jnp.einsum(
            "gqt,td->qgd",
            weights.astype(jnp.bfloat16),
            value_all,
            preferred_element_type=jnp.float32,
        )
        mixed = mixed / jnp.transpose(denom, (1, 0, 2))
        outputs.append(mixed.reshape(tile_rows, per_dev * HD).astype(jnp.bfloat16))
    return jnp.concatenate(outputs, axis=0)


def shards_body(
    query_rows,
    key_rows,
    value_rows,
    doc_of_block,
    expert_ids,
    gate_weights,
    norm_gain,
    w_in,
    w_down,
):
    seq_count = lax.axis_size("seq")
    tok_count = query_rows.shape[1]
    per_dev = QH // seq_count
    feat = per_dev * HD

    weights_local = jnp.concatenate([w_in, w_down[None]], axis=0).reshape(-1)
    weights_flat = lax.all_gather(weights_local, "seq", axis=0, tiled=True)
    weights_all = jnp.transpose(
        weights_flat.reshape((seq_count,) + (3,) + w_down.shape), (1, 0, 2, 3)
    ).reshape(3, seq_count * w_down.shape[0], w_down.shape[1])

    query_send = jnp.transpose(query_rows[0].reshape(tok_count, seq_count, feat), (1, 0, 2))
    kv_repeat = seq_count // KVH
    key_send = jnp.repeat(
        jnp.transpose(key_rows[0].reshape(tok_count, KVH, HD), (1, 0, 2)), kv_repeat, axis=0
    )
    value_send = jnp.repeat(
        jnp.transpose(value_rows[0].reshape(tok_count, KVH, HD), (1, 0, 2)), kv_repeat, axis=0
    )
    packed = jnp.concatenate([query_send, key_send, value_send], axis=2)
    packed_all = lax.all_to_all(packed, "seq", 0, 0, tiled=False)
    seq_length = seq_count * tok_count
    query_all = packed_all[:, :, :feat].reshape(seq_length, feat)
    key_all = packed_all[:, :, feat : feat + HD].reshape(seq_length, HD)
    value_all = packed_all[:, :, feat + HD :].reshape(seq_length, HD)

    token_doc = jnp.repeat(doc_of_block[0], BLK)
    attended = attend(query_all, key_all, value_all, token_doc, per_dev)
    attn_back = lax.all_to_all(
        attended.reshape(seq_count, tok_count, feat), "seq", 0, 0, tiled=False
    )
    attn_tokens = jnp.transpose(attn_back, (1, 0, 2)).reshape(tok_count, seq_count * feat)
    attn_float = attn_tokens.astype(jnp.float32)
    spread = jnp.mean(attn_float * attn_float, axis=-1, keepdims=True)
    normed = (attn_float * lax.rsqrt(spread + EPS) * norm_gain).astype(jnp.bfloat16)
    chosen = expert_ids[0] == 0
    routed = jnp.any(chosen, axis=-1)
    gate_share = jnp.sum(jnp.where(chosen, gate_weights[0], 0.0), axis=-1)
    slot_index = jnp.cumsum(routed.astype(jnp.int32)) - 1
    onehot = (slot_index[None, :] == jnp.arange(CAP, dtype=jnp.int32)[:, None]) & routed[None, :]
    dispatched = jnp.dot(
        onehot.astype(jnp.bfloat16), normed, preferred_element_type=jnp.float32
    ).astype(jnp.bfloat16)
    gathered = lax.all_gather(dispatched, "grp", axis=0, tiled=True)
    gate_up = jnp.einsum(
        "rd,kud->kru", gathered, weights_all[:2], preferred_element_type=jnp.float32
    )
    hidden = (jax.nn.silu(gate_up[0]) * gate_up[1]).astype(jnp.bfloat16)
    terms = jnp.einsum(
        "ru,ud->rd", hidden, weights_all[2], preferred_element_type=jnp.float32
    )
    returned = lax.psum_scatter(
        terms.astype(jnp.bfloat16), "grp", scatter_dimension=0, tiled=True
    )
    expert_out = jnp.dot(
        jnp.transpose(onehot).astype(jnp.bfloat16), returned, preferred_element_type=jnp.float32
    )
    layer_out = attn_float + gate_share[:, None] * expert_out
    return layer_out.astype(jnp.bfloat16)[None]


def solution(mesh):
    return jax.shard_map(
        shards_body,
        mesh=mesh,
        in_specs=(
            P("grp", "seq", None),
            P("grp", "seq", None),
            P("grp", "seq", None),
            P("grp", None),
            P("grp", "seq", None),
            P("grp", "seq", None),
            P(),
            P(None, ("seq", "grp"), None),
            P(("seq", "grp"), None),
        ),
        out_specs=P("grp", "seq", None),
        check_vma=False,
    )
```
